256 devices in a mesh: dp: 16 (over x, z_lo, core), space: 16 (over y, z_hi).
Axes of the slice: x: 4, y: 4, z: 8 (z_hi: 4, z_lo: 2; z = z_hi * 2 + z_lo), core: 2. Of those that a mesh axis runs over, the one named last changes fastest.
Arguments:
- acts_in: bfloat16 [16, 64, 64, 32, 128], P('dp', 'space'), may hold values from -6 to 6
- pre_act: bfloat16 [16, 64, 64, 32, 128], P('dp', 'space'), may hold values from -6 to 6
- weight_two: bfloat16 [128, 3, 3, 3, 128], P('space'), may hold values from -0.109375 to 0.109375
- grad_out: bfloat16 [16, 32, 32, 16, 128], P('dp', None, None, None, 'space'), may hold values from -6 to 6
Outputs:
- fine_grad: float32 [128, 3, 3, 3, 128], P('space')
- coarse_grad: float32 [128, 3, 3, 3, 128], P('space')
The draws below stay inside these ranges and needn't reach their ends.
All inputs are finite; a program needn't handle non-finite values.
Results may differ from the reference program's by a relative error of at most 0.003.
Values may be sent and summed in bfloat16 or wider, within the bound.
No kernel may reach another device: no remote copies, remote signals or barrier semaphores. Data moves between devices by JAX's collectives and lax.ppermute only.
A program may use at most 128 MiB of HBM per device.

```python
import math
import jax
import jax.numpy as jnp
from jax import lax

C = 128
NY = 64
NZ = 32
SAMPLES = 16
NX = 64


def raised(result, key, source, target, shards_of, factor):
    def block_of(position):
        return (jnp.arange(result.shape[position]) // (result.shape[position] // shards_of)).reshape((-1,) + (1,) * (result.ndim - 1 - position))

    near = jax.random.permutation(key, shards_of)[block_of(target)]
    far = (block_of(target) + shards_of // 2) % shards_of
    return jnp.where((block_of(source) == near) | (block_of(source) == far), factor * result, result)


def level_of(stream_key, extent, split, least, top_value):
    factor_of = 1.0
    for dim, blocks in split:
        draws = jax.random.uniform(jax.random.fold_in(jax.random.fold_in(stream_key, 6), dim), (blocks,), jnp.float32, least / len(split), top_value / len(split))
        factor_of = factor_of * jnp.repeat(jnp.exp(draws), extent[dim] // blocks).reshape((-1,) + (1,) * (len(extent) - 1 - dim))
    return factor_of


def noise(own_key, extent, deviation, bound, cuts=(), held_as=jnp.bfloat16):
    gain = level_of(own_key, extent, cuts, -0.22, 0.18) if cuts else 1.0
    array = jax.random.normal(own_key, extent, jnp.float32) * deviation * gain
    return jnp.minimum(jnp.maximum(array, -bound), bound).astype(held_as)


def heavy_noise(own_key, dims, deviation, bound, cuts, heavy, kind=jnp.bfloat16):
    drawn = deviation * jax.random.normal(own_key, dims, jnp.float32)
    if cuts:
        drawn = drawn * level_of(own_key, dims, cuts, -0.22, 0.18)
    return jnp.clip(raised(drawn, jax.random.fold_in(own_key, 3), *heavy), -bound, bound).astype(kind)


def setup_inputs(seed: int = 0) -> dict:
    seeds = jax.random.split(jax.random.key(seed), 5)
    return {
        "acts_in": noise(seeds[0], (SAMPLES, NX, NY, NZ, C), 1.0, 6.0, ((0, 16), (1, 16))),
        "pre_act": heavy_noise(seeds[1], (SAMPLES, NX, NY, NZ, C), 1.0, 6.0, ((0, 16), (1, 16)), (1, 4, 16, 2.0)),
        "weight_two": noise(seeds[2], (C, 3, 3, 3, C), (27 * C) ** -0.5, 0.109375, ((0, 16),)),
        "grad_out": noise(seeds[3], (SAMPLES, NX // 2, NY // 2, NZ // 2, C), 1.0, 6.0, ((0, 16), (4, 16))),
    }


leak_slope = 0.3
parity_taps = {0: ((1, 0),), 1: ((0, 1), (2, 0))}

def transpose_conv(padded, weight):
    rows_x = padded.shape[0] - 1
    rows_y = padded.shape[1] - 1
    rows_z = padded.shape[2] - 1
    classes = []
    for parity_x in (0, 1):
        for parity_y in (0, 1):
            for parity_z in (0, 1):
                pieces = []
                blocks = []
                for tap_x, move_x in parity_taps[parity_x]:
                    for tap_y, move_y in parity_taps[parity_y]:
                        for tap_z, move_z in parity_taps[parity_z]:
                            pieces.append(padded[move_x:move_x + rows_x, move_y:move_y + rows_y, move_z:move_z + rows_z, :])
                            blocks.append(weight[:, tap_x, tap_y, tap_z, :])
                stacked = jnp.concatenate(pieces, axis=3)
                flat = stacked.reshape(-1, stacked.shape[3])
                mixing = jnp.concatenate(blocks, axis=0)
                classes.append(jnp.dot(flat, mixing, preferred_element_type=jnp.float32))
    outputs = weight.shape[4]
    joined = jnp.stack(classes).reshape(2, 2, 2, rows_x, rows_y, rows_z, outputs)
    joined = joined.transpose(3, 0, 4, 1, 5, 2, 6)
    return joined.reshape(2 * rows_x, 2 * rows_y, 2 * rows_z, outputs)

def weight_terms(source, gradient, stride):
    count_x, count_y, count_z, filters = gradient.shape
    flat_grad = gradient.reshape(-1, filters)
    terms = []
    for tap_x in range(3):
        for tap_y in range(3):
            for tap_z in range(3):
                piece = source[tap_x:tap_x + stride * count_x:stride, tap_y:tap_y + stride * count_y:stride, tap_z:tap_z + stride * count_z:stride, :]
                terms.append(lax.dot_general(flat_grad, piece.reshape(-1, piece.shape[3]), (((0,), (0,)), ((), ())), preferred_element_type=jnp.float32))
    return jnp.stack(terms, axis=1).reshape(filters, 3, 3, 3, source.shape[3])

def reference(acts_in, pre_act, weight_two, grad_out):
    scaling = 1.0 / math.sqrt(SAMPLES * NX * NY * NZ)

    def sample_step(carry, items):
        acts, before, cotangent = items
        before_f = before.astype(jnp.float32)
        hidden = jnp.where(before_f > 0, before_f, leak_slope * before_f).astype(jnp.bfloat16)
        lower = jnp.pad(hidden, ((1, 0), (1, 0), (1, 0), (0, 0)))
        coarse = weight_terms(lower, cotangent, 2)
        upper = jnp.pad(cotangent, ((0, 1), (0, 1), (0, 1), (0, 0)))
        back = transpose_conv(upper, weight_two)
        delta = (back * jnp.where(before_f > 0, 1.0, leak_slope)).astype(jnp.bfloat16)
        framed = jnp.pad(acts, ((1, 1), (1, 1), (1, 1), (0, 0)))
        fine = weight_terms(framed, delta, 1)
        return ((carry[0] + fine, carry[1] + coarse), None)
    zeros = jnp.zeros((C, 3, 3, 3, C), jnp.float32)
    totals, unused = lax.scan(sample_step, (zeros, zeros), (acts_in, pre_act, grad_out))
    return (totals[0] * scaling, totals[1] * scaling)
```

```python
import math

import jax
import jax.numpy as jnp
from jax import lax
from jax.sharding import PartitionSpec as P

leak_slope = 0.3
parity_taps = {0: ((1, 0),), 1: ((0, 1), (2, 0))}


def passed_along(block, axis, distance):
    devices = range(lax.axis_size(axis))
    route = [(i - distance, i) for i in devices if i - distance in devices]
    return lax.ppermute(block, axis, route)


def padded_2(shard, sides, width):
    for axis, dim in sides:
        size, length = (lax.axis_size(axis), shard.shape[dim])
        up = [(i, (i + 1) % size) for i in range(size - 1)]
        down = [(j, i) for i, j in up]
        last = lax.slice_in_dim(shard, length - width, length, axis=dim)
        initial = lax.slice_in_dim(shard, 0, width, axis=dim)
        before = lax.ppermute(last, axis, up)
        after = lax.ppermute(initial, axis, down)
        shard = jnp.concatenate([before, shard, after], axis=dim)
    return shard


def transpose_conv(padded, weight):
    rows_x = padded.shape[0] - 1
    rows_y = padded.shape[1] - 1
    rows_z = padded.shape[2] - 1
    outputs = weight.shape[4]
    zpair = jnp.concatenate([padded[:, :, :rows_z, :], padded[:, :, 1:, :]], axis=3)
    nothing = jnp.zeros((weight.shape[0], outputs), weight.dtype)
    classes = []
    for parity_x in (0, 1):
        for parity_y in (0, 1):
            pieces = []
            blocks = []
            for tap_x, move_x in parity_taps[parity_x]:
                for tap_y, move_y in parity_taps[parity_y]:
                    pieces.append(zpair[move_x : move_x + rows_x, move_y : move_y + rows_y])
                    taps = weight[:, tap_x, tap_y]
                    first = jnp.concatenate([taps[:, 1], taps[:, 2]], axis=1)
                    second = jnp.concatenate([nothing, taps[:, 0]], axis=1)
                    blocks.append(jnp.concatenate([first, second], axis=0))
            stacked = jnp.concatenate(pieces, axis=3)
            flat = stacked.reshape(-1, stacked.shape[3])
            mixing = jnp.concatenate(blocks, axis=0)
            classes.append(jnp.dot(flat, mixing, preferred_element_type=jnp.float32))
    joined = jnp.stack(classes).reshape(2, 2, rows_x, rows_y, rows_z, 2 * outputs)
    joined = joined.transpose(2, 0, 3, 1, 4, 5)
    return joined.reshape(2 * rows_x, 2 * rows_y, 2 * rows_z, outputs)


def depth_taps(volume):
    count_x, count_y, count_z, channels = volume.shape
    paired = volume.reshape(count_x, count_y, count_z // 2, 2 * channels)
    even = paired[..., :channels]
    odd = paired[..., channels:]
    earlier = jnp.pad(odd[:, :, :-1, :], ((0, 0), (0, 0), (1, 0), (0, 0)))
    return jnp.concatenate([earlier, even, odd], axis=3)


def coarse_terms(hidden, below, gradient):
    count_x, count_y, count_z, filters = gradient.shape
    flat_grad = gradient.reshape(-1, filters)
    stacked = depth_taps(hidden)
    width = stacked.shape[3]
    split = stacked.reshape(count_x, 2, count_y, 2, count_z, width)
    rim = depth_taps(below).reshape(1, count_y, 2, count_z, width)
    by_x = [jnp.concatenate([rim, split[:-1, 1]], axis=0), split[:, 0], split[:, 1]]
    terms = []
    for tap_x in range(3):
        plane = by_x[tap_x]
        by_y = [
            jnp.pad(plane[:, :-1, 1], ((0, 0), (1, 0), (0, 0), (0, 0))),
            plane[:, :, 0],
            plane[:, :, 1],
        ]
        for tap_y in range(3):
            piece = by_y[tap_y].reshape(-1, width)
            terms.append(
                lax.dot_general(
                    flat_grad, piece, (((0,), (0,)), ((), ())), preferred_element_type=jnp.float32
                )
            )
    return jnp.stack(terms, axis=1).reshape(filters, 3, 3, 3, width // 3)


def fine_terms(framed, gradient):
    count_x, count_y, count_z, filters = gradient.shape
    flat_grad = gradient.reshape(-1, filters)
    stacked = jnp.concatenate(
        [framed[:, :, shift : shift + count_z, :] for shift in range(3)], axis=3
    )
    width = stacked.shape[3]
    terms = []
    for tap_x in range(3):
        for tap_y in range(3):
            piece = stacked[tap_x : tap_x + count_x, tap_y : tap_y + count_y].reshape(-1, width)
            terms.append(
                lax.dot_general(
                    flat_grad, piece, (((0,), (0,)), ((), ())), preferred_element_type=jnp.float32
                )
            )
    return jnp.stack(terms, axis=1).reshape(filters, 3, 3, 3, width // 3)


def space_share(whole_terms, parts):
    blocks = whole_terms.reshape((parts, -1) + whole_terms.shape[1:])
    arrived = lax.all_to_all(blocks, "space", split_axis=0, concat_axis=0, tiled=True)
    return arrived.sum(axis=0)


def dp_total(share, groups):
    pieces = share.reshape(groups, -1)
    mine = lax.all_to_all(pieces, "dp", split_axis=0, concat_axis=0, tiled=True).sum(axis=0)
    copies = jnp.broadcast_to(mine[None], pieces.shape)
    whole = lax.all_to_all(copies, "dp", split_axis=0, concat_axis=0, tiled=True)
    return whole.reshape(share.shape)


def gathered(block, axis):
    size = lax.axis_size(axis)
    copies = jnp.broadcast_to(block[None], (size,) + block.shape)
    whole = lax.all_to_all(copies, axis, split_axis=0, concat_axis=0, tiled=True)
    return whole.reshape((size * block.shape[0],) + block.shape[1:])


def body(acts_in, pre_act, weight_two, grad_out):
    parts = lax.axis_size("space")
    groups = lax.axis_size("dp")
    acts = acts_in[0]
    depth, across, height, channels = acts.shape
    scaling = 1.0 / math.sqrt(groups * depth * parts * across * height)
    before_f = pre_act[0].astype(jnp.float32)
    hidden = jnp.where(before_f > 0, before_f, leak_slope * before_f).astype(jnp.bfloat16)
    grad_tile = lax.all_to_all(grad_out, "space", split_axis=1, concat_axis=4, tiled=True)[0]
    below = passed_along(hidden[-1:], "space", 1)
    whole_weight = gathered(weight_two, "space")
    above = passed_along(grad_tile[:1], "space", -1)
    upper = jnp.pad(jnp.concatenate([grad_tile, above], axis=0), ((0, 0), (0, 1), (0, 1), (0, 0)))
    back = transpose_conv(upper, whole_weight)
    delta = (back * jnp.where(before_f > 0, 1.0, leak_slope)).astype(jnp.bfloat16)
    framed = padded_2(acts, (("space", 0),), 1)
    framed = jnp.pad(framed, ((0, 0), (1, 1), (1, 1), (0, 0)))
    coarse_full = coarse_terms(hidden, below, grad_tile)
    fine_full = fine_terms(framed, delta)
    filters = fine_full.shape[0]
    both = jnp.stack([fine_full.reshape(filters, -1), coarse_full.reshape(filters, -1)], axis=1)
    share = space_share(both, parts)
    share = dp_total(share, groups)
    shape = (share.shape[0],) + fine_full.shape[1:]
    return (share[:, 0].reshape(shape) * scaling, share[:, 1].reshape(shape) * scaling)


def solution(mesh):
    placed = (
        P("dp", "space", None, None, None),
        P("dp", "space", None, None, None),
        P("space", None, None, None, None),
        P("dp", None, None, None, "space"),
    )
    return jax.shard_map(
        body,
        mesh=mesh,
        in_specs=placed,
        out_specs=(P("space", None, None, None, None), P("space", None, None, None, None)),
        check_vma=False,
    )
```

```python
import math

import jax
import jax.numpy as jnp
from jax import lax
from jax.sharding import PartitionSpec as P

leak_slope = 0.3
parity_taps = {0: ((1, 0),), 1: ((0, 1), (2, 0))}


def passed_along(block, axis, distance):
    devices = range(lax.axis_size(axis))
    route = [(i - distance, i) for i in devices if i - distance in devices]
    return lax.ppermute(block, axis, route)


def padded_2(shard, sides, width):
    for axis, dim in sides:
        size, length = (lax.axis_size(axis), shard.shape[dim])
        up = [(i, (i + 1) % size) for i in range(size - 1)]
        down = [(j, i) for i, j in up]
        last = lax.slice_in_dim(shard, length - width, length, axis=dim)
        initial = lax.slice_in_dim(shard, 0, width, axis=dim)
        before = lax.ppermute(last, axis, up)
        after = lax.ppermute(initial, axis, down)
        shard = jnp.concatenate([before, shard, after], axis=dim)
    return shard


def transpose_conv(padded, weight):
    rows_x = padded.shape[0] - 1
    rows_y = padded.shape[1] - 1
    rows_z = padded.shape[2] - 1
    outputs = weight.shape[4]
    zpair = jnp.concatenate([padded[:, :, :rows_z, :], padded[:, :, 1:, :]], axis=3)
    nothing = jnp.zeros((weight.shape[0], outputs), weight.dtype)
    classes = []
    for parity_x in (0, 1):
        for parity_y in (0, 1):
            pieces = []
            blocks = []
            for tap_x, move_x in parity_taps[parity_x]:
                for tap_y, move_y in parity_taps[parity_y]:
                    pieces.append(zpair[move_x : move_x + rows_x, move_y : move_y + rows_y])
                    taps = weight[:, tap_x, tap_y]
                    first = jnp.concatenate([taps[:, 1], taps[:, 2]], axis=1)
                    second = jnp.concatenate([nothing, taps[:, 0]], axis=1)
                    blocks.append(jnp.concatenate([first, second], axis=0))
            stacked = jnp.concatenate(pieces, axis=3)
            flat = stacked.reshape(-1, stacked.shape[3])
            mixing = jnp.concatenate(blocks, axis=0)
            classes.append(jnp.dot(flat, mixing, preferred_element_type=jnp.float32))
    joined = jnp.stack(classes).reshape(2, 2, rows_x, rows_y, rows_z, 2 * outputs)
    joined = joined.transpose(2, 0, 3, 1, 4, 5)
    return joined.reshape(2 * rows_x, 2 * rows_y, 2 * rows_z, outputs)


def depth_taps(volume):
    count_x, count_y, count_z, channels = volume.shape
    paired = volume.reshape(count_x, count_y, count_z // 2, 2 * channels)
    even = paired[..., :channels]
    odd = paired[..., channels:]
    earlier = jnp.pad(odd[:, :, :-1, :], ((0, 0), (0, 0), (1, 0), (0, 0)))
    return jnp.concatenate([earlier, even, odd], axis=3)


def coarse_terms(hidden, below, gradient):
    count_x, count_y, count_z, filters = gradient.shape
    flat_grad = gradient.reshape(-1, filters)
    stacked = depth_taps(hidden)
    width = stacked.shape[3]
    split = stacked.reshape(count_x, 2, count_y, 2, count_z, width)
    rim = depth_taps(below).reshape(1, count_y, 2, count_z, width)
    by_x = [jnp.concatenate([rim, split[:-1, 1]], axis=0), split[:, 0], split[:, 1]]
    terms = []
    for tap_x in range(3):
        plane = by_x[tap_x]
        by_y = [
            jnp.pad(plane[:, :-1, 1], ((0, 0), (1, 0), (0, 0), (0, 0))),
            plane[:, :, 0],
            plane[:, :, 1],
        ]
        for tap_y in range(3):
            piece = by_y[tap_y].reshape(-1, width)
            terms.append(
                lax.dot_general(
                    flat_grad, piece, (((0,), (0,)), ((), ())), preferred_element_type=jnp.float32
                )
            )
    return jnp.stack(terms, axis=1).reshape(filters, 3, 3, 3, width // 3)


def fine_terms(framed, gradient):
    count_x, count_y, count_z, filters = gradient.shape
    flat_grad = gradient.reshape(-1, filters)
    stacked = jnp.concatenate(
        [framed[:, :, shift : shift + count_z, :] for shift in range(3)], axis=3
    )
    width = stacked.shape[3]
    terms = []
    for tap_x in range(3):
        for tap_y in range(3):
            piece = stacked[tap_x : tap_x + count_x, tap_y : tap_y + count_y].reshape(-1, width)
            terms.append(
                lax.dot_general(
                    flat_grad, piece, (((0,), (0,)), ((), ())), preferred_element_type=jnp.float32
                )
            )
    return jnp.stack(terms, axis=1).reshape(filters, 3, 3, 3, width // 3)


def space_share(whole_terms, parts):
    blocks = whole_terms.reshape((parts, -1) + whole_terms.shape[1:])
    arrived = lax.all_to_all(blocks, "space", split_axis=0, concat_axis=0, tiled=True)
    return arrived.sum(axis=0)


def dp_total(share, groups, core):
    rows, width = share.shape
    pieces = share.reshape(groups // 2, 1, -1)
    same_core = (jnp.arange(2) == core)[None, :, None]
    outgoing = jnp.where(same_core, pieces, 0.0).reshape(groups, -1)
    mine = lax.all_to_all(outgoing, "dp", split_axis=0, concat_axis=0, tiled=True).sum(axis=0)
    copies = jnp.broadcast_to(mine[None], outgoing.shape)
    whole = lax.all_to_all(copies, "dp", split_axis=0, concat_axis=0, tiled=True)
    return whole.reshape(groups // 2, 2, rows * width // (groups // 2))


def gathered(block, axis):
    size = lax.axis_size(axis)
    copies = jnp.broadcast_to(block[None], (size,) + block.shape)
    whole = lax.all_to_all(copies, axis, split_axis=0, concat_axis=0, tiled=True)
    return whole.reshape((size * block.shape[0],) + block.shape[1:])


def body(acts_in, pre_act, weight_two, grad_out):
    parts = lax.axis_size("space")
    groups = lax.axis_size("dp")
    acts = acts_in[0]
    depth, across, height, channels = acts.shape
    scaling = 1.0 / math.sqrt(groups * depth * parts * across * height)
    before_f = pre_act[0].astype(jnp.float32)
    hidden = jnp.where(before_f > 0, before_f, leak_slope * before_f).astype(jnp.bfloat16)
    grad_tile = lax.all_to_all(grad_out, "space", split_axis=1, concat_axis=4, tiled=True)[0]
    below = passed_along(hidden[-1:], "space", 1)
    whole_weight = gathered(weight_two, "space")
    above = passed_along(grad_tile[:1], "space", -1)
    upper = jnp.pad(jnp.concatenate([grad_tile, above], axis=0), ((0, 0), (0, 1), (0, 1), (0, 0)))
    back = transpose_conv(upper, whole_weight)
    delta = (back * jnp.where(before_f > 0, 1.0, leak_slope)).astype(jnp.bfloat16)
    framed = padded_2(acts, (("space", 0),), 1)
    framed = jnp.pad(framed, ((0, 0), (1, 1), (1, 1), (0, 0)))
    coarse_full = coarse_terms(hidden, below, grad_tile)
    fine_full = fine_terms(framed, delta)
    filters = fine_full.shape[0]
    fine_flat = fine_full.reshape(filters, -1)
    coarse_flat = coarse_full.reshape(filters, -1)
    core = lax.axis_index("dp") % 2
    kept = jnp.where(core == 0, fine_flat, coarse_flat)
    given = jnp.where(core == 0, coarse_flat, fine_flat)
    partner = [(i, i ^ 1) for i in range(groups)]
    pair_sum = kept + lax.ppermute(given, "dp", partner)
    share = space_share(pair_sum, parts)
    share = dp_total(share, groups, core)
    shape = (share.shape[0],) + fine_full.shape[1:]
    return (share[:, 0].reshape(shape) * scaling, share[:, 1].reshape(shape) * scaling)


def solution(mesh):
    placed = (
        P("dp", "space", None, None, None),
        P("dp", "space", None, None, None),
        P("space", None, None, None, None),
        P("dp", None, None, None, "space"),
    )
    return jax.shard_map(
        body,
        mesh=mesh,
        in_specs=placed,
        out_specs=(P("space", None, None, None, None), P("space", None, None, None, None)),
        check_vma=False,
    )
```

```python
import math

import jax
import jax.numpy as jnp
from jax import lax
from jax.sharding import PartitionSpec as P


leak_slope = 0.3
parity_taps = {0: ((1, 0),), 1: ((0, 1), (2, 0))}


def passed_along(block, axis, distance):
    devices = range(lax.axis_size(axis))
    route = [(i - distance, i) for i in devices if i - distance in devices]
    return lax.ppermute(block, axis, route)


def padded_2(shard, sides, width):
    for axis, dim in sides:
        size, length = (lax.axis_size(axis), shard.shape[dim])
        up = [(i, (i + 1) % size) for i in range(size - 1)]
        down = [(j, i) for i, j in up]
        last = lax.slice_in_dim(shard, length - width, length, axis=dim)
        initial = lax.slice_in_dim(shard, 0, width, axis=dim)
        before = lax.ppermute(last, axis, up)
        after = lax.ppermute(initial, axis, down)
        shard = jnp.concatenate([before, shard, after], axis=dim)
    return shard


def transpose_conv(padded, weight):
    rows_x = padded.shape[0] - 1
    rows_y = padded.shape[1] - 1
    rows_z = padded.shape[2] - 1
    outputs = weight.shape[4]
    zpair = jnp.concatenate([padded[:, :, :rows_z, :], padded[:, :, 1:, :]], axis=3)
    nothing = jnp.zeros((weight.shape[0], outputs), weight.dtype)
    classes = []
    for parity_x in (0, 1):
        for parity_y in (0, 1):
            pieces = []
            blocks = []
            for tap_x, move_x in parity_taps[parity_x]:
                for tap_y, move_y in parity_taps[parity_y]:
                    pieces.append(zpair[move_x : move_x + rows_x, move_y : move_y + rows_y])
                    taps = weight[:, tap_x, tap_y]
                    first = jnp.concatenate([taps[:, 1], taps[:, 2]], axis=1)
                    second = jnp.concatenate([nothing, taps[:, 0]], axis=1)
                    blocks.append(jnp.concatenate([first, second], axis=0))
            stacked = jnp.concatenate(pieces, axis=3)
            flat = stacked.reshape(-1, stacked.shape[3])
            mixing = jnp.concatenate(blocks, axis=0)
            classes.append(jnp.dot(flat, mixing, preferred_element_type=jnp.float32))
    joined = jnp.stack(classes).reshape(2, 2, rows_x, rows_y, rows_z, 2 * outputs)
    joined = joined.transpose(2, 0, 3, 1, 4, 5)
    return joined.reshape(2 * rows_x, 2 * rows_y, 2 * rows_z, outputs)


def depth_taps(volume):
    count_x, count_y, count_z, channels = volume.shape
    paired = volume.reshape(count_x, count_y, count_z // 2, 2 * channels)
    even = paired[..., :channels]
    odd = paired[..., channels:]
    earlier = jnp.pad(odd[:, :, :-1, :], ((0, 0), (0, 0), (1, 0), (0, 0)))
    return jnp.concatenate([earlier, even, odd], axis=3)


def coarse_terms(hidden, below, gradient):
    count_x, count_y, count_z, filters = gradient.shape
    flat_grad = gradient.reshape(-1, filters)
    stacked = depth_taps(hidden)
    width = stacked.shape[3]
    split = stacked.reshape(count_x, 2, count_y, 2, count_z, width)
    rim = depth_taps(below).reshape(1, count_y, 2, count_z, width)
    by_x = [jnp.concatenate([rim, split[:-1, 1]], axis=0), split[:, 0], split[:, 1]]
    terms = []
    for tap_x in range(3):
        plane = by_x[tap_x]
        by_y = [
            jnp.pad(plane[:, :-1, 1], ((0, 0), (1, 0), (0, 0), (0, 0))),
            plane[:, :, 0],
            plane[:, :, 1],
        ]
        for tap_y in range(3):
            piece = by_y[tap_y].reshape(-1, width)
            terms.append(
                lax.dot_general(
                    flat_grad, piece, (((0,), (0,)), ((), ())), preferred_element_type=jnp.float32
                )
            )
    return jnp.stack(terms, axis=1).reshape(filters, 3, 3, 3, width // 3)


def fine_terms(framed, gradient):
    count_x, count_y, count_z, filters = gradient.shape
    flat_grad = gradient.reshape(-1, filters)
    stacked = jnp.concatenate(
        [framed[:, :, shift : shift + count_z, :] for shift in range(3)], axis=3
    )
    width = stacked.shape[3]
    terms = []
    for tap_x in range(3):
        for tap_y in range(3):
            piece = stacked[tap_x : tap_x + count_x, tap_y : tap_y + count_y].reshape(-1, width)
            terms.append(
                lax.dot_general(
                    flat_grad, piece, (((0,), (0,)), ((), ())), preferred_element_type=jnp.float32
                )
            )
    return jnp.stack(terms, axis=1).reshape(filters, 3, 3, 3, width // 3)


def pair_sum(terms, core, groups):
    halves = terms.reshape(terms.shape[0], 2, -1)
    kept = jnp.where(core == 0, halves[:, 0], halves[:, 1])
    given = jnp.where(core == 0, halves[:, 1], halves[:, 0])
    partner = [(i, i ^ 1) for i in range(groups)]
    return kept + lax.ppermute(given, "dp", partner)


def space_share(whole_terms, parts):
    blocks = whole_terms.reshape((parts, -1) + whole_terms.shape[1:])
    arrived = lax.all_to_all(blocks, "space", split_axis=0, concat_axis=0, tiled=True)
    return arrived.sum(axis=0)


def dp_total(share, groups, core):
    rows, width = share.shape
    pieces = share.reshape(groups // 2, 1, -1)
    same_core = (jnp.arange(2) == core)[None, :, None]
    outgoing = jnp.where(same_core, pieces, 0.0).reshape(groups, -1)
    mine = lax.all_to_all(outgoing, "dp", split_axis=0, concat_axis=0, tiled=True).sum(axis=0)
    copies = jnp.broadcast_to(mine[None], outgoing.shape)
    whole = lax.all_to_all(copies, "dp", split_axis=0, concat_axis=0, tiled=True)
    return whole.reshape(groups // 2, 2, rows * width // (groups // 2))


def gathered(block, axis):
    size = lax.axis_size(axis)
    copies = jnp.broadcast_to(block[None], (size,) + block.shape)
    whole = lax.all_to_all(copies, axis, split_axis=0, concat_axis=0, tiled=True)
    return whole.reshape((size * block.shape[0],) + block.shape[1:])


def staged(acts_in, pre_act, weight_two, grad_out):
    parts = lax.axis_size("space")
    groups = lax.axis_size("dp")
    acts = acts_in[0]
    depth, across, height, _ = acts.shape
    scaling = 1.0 / math.sqrt(groups * depth * parts * across * height)
    before_f = pre_act[0].astype(jnp.float32)
    hidden = jnp.where(before_f > 0, before_f, leak_slope * before_f).astype(jnp.bfloat16)
    hidden = lax.optimization_barrier(hidden)
    grad_tile = lax.all_to_all(grad_out, "space", split_axis=1, concat_axis=4, tiled=True)[0]
    below = passed_along(hidden[-1:], "space", 1)
    whole_weight = gathered(weight_two, "space")
    above = passed_along(grad_tile[:1], "space", -1)
    upper = jnp.pad(jnp.concatenate([grad_tile, above], axis=0), ((0, 0), (0, 1), (0, 1), (0, 0)))
    core = lax.axis_index("dp") % 2
    coarse_full = coarse_terms(hidden, below, grad_tile)
    coarse_pair = pair_sum(coarse_full, core, groups)
    coarse_share = space_share(coarse_pair, parts)
    back = transpose_conv(upper, whole_weight)
    delta = (back * jnp.where(hidden > 0, 1.0, leak_slope)).astype(jnp.bfloat16)
    framed = padded_2(acts, (("space", 0),), 1)
    framed = jnp.pad(framed, ((0, 0), (1, 1), (1, 1), (0, 0)))
    fine_full = fine_terms(framed, delta)
    fine_share = space_share(pair_sum(fine_full, core, groups), parts)
    both = jnp.stack([fine_share, coarse_share], axis=1)
    total = dp_total(both.reshape(both.shape[0], -1), groups, core)
    rows = total.shape[0]
    total = total.reshape(rows, 2, 2, -1)
    shape = (rows,) + fine_full.shape[1:]
    fine_sum = total[:, :, 0].reshape(shape)
    coarse_sum = total[:, :, 1].reshape(shape)
    return (fine_sum * scaling, coarse_sum * scaling)


def solution(mesh):
    placed = (
        P("dp", "space", None, None, None),
        P("dp", "space", None, None, None),
        P("space", None, None, None, None),
        P("dp", None, None, None, "space"),
    )
    return jax.shard_map(
        staged,
        mesh=mesh,
        in_specs=placed,
        out_specs=(P("space", None, None, None, None), P("space", None, None, None, None)),
        check_vma=False,
    )
```

```python
import math

import jax
import jax.numpy as jnp
from jax import lax
from jax.sharding import PartitionSpec as P


leak_slope = 0.3


def passed_along(block, axis, distance):
    devices = range(lax.axis_size(axis))
    route = [(i - distance, i) for i in devices if i - distance in devices]
    return lax.ppermute(block, axis, route)


def padded_2(shard, sides, width):
    for axis, dim in sides:
        size, length = (lax.axis_size(axis), shard.shape[dim])
        up = [(i, (i + 1) % size) for i in range(size - 1)]
        down = [(j, i) for i, j in up]
        last = lax.slice_in_dim(shard, length - width, length, axis=dim)
        initial = lax.slice_in_dim(shard, 0, width, axis=dim)
        before = lax.ppermute(last, axis, up)
        after = lax.ppermute(initial, axis, down)
        shard = jnp.concatenate([before, shard, after], axis=dim)
    return shard


WEIGHT_GRAD = lax.ConvDimensionNumbers((4, 0, 1, 2, 3), (4, 0, 1, 2, 3), (4, 0, 1, 2, 3))
INPUT_GRAD = lax.ConvDimensionNumbers((0, 4, 1, 2, 3), (4, 0, 1, 2, 3), (0, 4, 1, 2, 3))


def fine_conv(framed, gradient):
    return lax.conv_general_dilated(
        framed[None], gradient[None], (1, 1, 1), "VALID",
        dimension_numbers=WEIGHT_GRAD, preferred_element_type=jnp.float32,
    )


def coarse_conv(hidden, below, gradient):
    lower = jnp.concatenate([below, hidden], axis=0)
    lower = jnp.pad(lower, ((0, 0), (1, 0), (1, 0), (0, 0)))
    return lax.conv_general_dilated(
        lower[None], gradient[None], (1, 1, 1), "VALID", rhs_dilation=(2, 2, 2),
        dimension_numbers=WEIGHT_GRAD, preferred_element_type=jnp.float32,
    )


def transpose_native(upper, weight):
    flipped = jnp.flip(weight, axis=(1, 2, 3))
    back = lax.conv_general_dilated(
        upper[None], flipped, (1, 1, 1), ((1, 0), (1, 2), (1, 2)), lhs_dilation=(2, 2, 2),
        dimension_numbers=INPUT_GRAD, preferred_element_type=jnp.float32,
    )
    return back[0]


def pair_sum(terms, core, groups):
    halves = terms.reshape(terms.shape[0], 2, -1)
    kept = jnp.where(core == 0, halves[:, 0], halves[:, 1])
    given = jnp.where(core == 0, halves[:, 1], halves[:, 0])
    partner = [(i, i ^ 1) for i in range(groups)]
    return kept + lax.ppermute(given, "dp", partner)


def space_share(whole_terms, parts):
    blocks = whole_terms.reshape((parts, -1) + whole_terms.shape[1:])
    arrived = lax.all_to_all(blocks, "space", split_axis=0, concat_axis=0, tiled=True)
    return arrived.sum(axis=0)


def dp_total(share, groups, core):
    rows, width = share.shape
    pieces = share.reshape(groups // 2, 1, -1)
    same_core = (jnp.arange(2) == core)[None, :, None]
    outgoing = jnp.where(same_core, pieces, 0.0).reshape(groups, -1)
    mine = lax.all_to_all(outgoing, "dp", split_axis=0, concat_axis=0, tiled=True).sum(axis=0)
    copies = jnp.broadcast_to(mine[None], outgoing.shape)
    whole = lax.all_to_all(copies, "dp", split_axis=0, concat_axis=0, tiled=True)
    return whole.reshape(groups // 2, 2, rows * width // (groups // 2))


def gathered(block, axis):
    size = lax.axis_size(axis)
    copies = jnp.broadcast_to(block[None], (size,) + block.shape)
    whole = lax.all_to_all(copies, axis, split_axis=0, concat_axis=0, tiled=True)
    return whole.reshape((size * block.shape[0],) + block.shape[1:])


def staged(acts_in, pre_act, weight_two, grad_out):
    parts = lax.axis_size("space")
    groups = lax.axis_size("dp")
    acts = acts_in[0]
    depth, across, height, _ = acts.shape
    scaling = 1.0 / math.sqrt(groups * depth * parts * across * height)
    before_f = pre_act[0].astype(jnp.float32)
    hidden = jnp.where(before_f > 0, before_f, leak_slope * before_f).astype(jnp.bfloat16)
    hidden = lax.optimization_barrier(hidden)
    grad_tile = lax.all_to_all(grad_out, "space", split_axis=1, concat_axis=4, tiled=True)[0]
    below = passed_along(hidden[-1:], "space", 1)
    whole_weight = gathered(weight_two, "space")
    above = passed_along(grad_tile[:1], "space", -1)
    upper = jnp.concatenate([grad_tile, above], axis=0)
    core = lax.axis_index("dp") % 2
    coarse_full = coarse_conv(hidden, below, grad_tile)
    coarse_pair = pair_sum(coarse_full, core, groups)
    coarse_share = space_share(coarse_pair, parts)
    back = transpose_native(upper, whole_weight)
    delta = (back * jnp.where(hidden > 0, 1.0, leak_slope)).astype(jnp.bfloat16)
    framed = padded_2(acts, (("space", 0),), 1)
    framed = jnp.pad(framed, ((0, 0), (1, 1), (1, 1), (0, 0)))
    fine_full = fine_conv(framed, delta)
    fine_share = space_share(pair_sum(fine_full, core, groups), parts)
    both = jnp.stack([fine_share, coarse_share], axis=1)
    total = dp_total(both.reshape(both.shape[0], -1), groups, core)
    rows = total.shape[0]
    total = total.reshape(rows, 2, 2, -1)
    shape = (rows,) + fine_full.shape[1:]
    fine_sum = total[:, :, 0].reshape(shape)
    coarse_sum = total[:, :, 1].reshape(shape)
    return (fine_sum * scaling, coarse_sum * scaling)


def solution(mesh):
    placed = (
        P("dp", "space", None, None, None),
        P("dp", "space", None, None, None),
        P("space", None, None, None, None),
        P("dp", None, None, None, "space"),
    )
    return jax.shard_map(
        staged,
        mesh=mesh,
        in_specs=placed,
        out_specs=(P("space", None, None, None, None), P("space", None, None, None, None)),
        check_vma=False,
    )
```

```python
import math

import jax
import jax.numpy as jnp
from jax import lax
from jax.sharding import PartitionSpec as P


leak_slope = 0.3
parity_taps = {0: ((1, 0),), 1: ((0, 1), (2, 0))}


def passed_along(block, axis, distance):
    devices = range(lax.axis_size(axis))
    route = [(i - distance, i) for i in devices if i - distance in devices]
    return lax.ppermute(block, axis, route)


def padded_2(shard, sides, width):
    for axis, dim in sides:
        size, length = (lax.axis_size(axis), shard.shape[dim])
        up = [(i, (i + 1) % size) for i in range(size - 1)]
        down = [(j, i) for i, j in up]
        last = lax.slice_in_dim(shard, length - width, length, axis=dim)
        initial = lax.slice_in_dim(shard, 0, width, axis=dim)
        before = lax.ppermute(last, axis, up)
        after = lax.ppermute(initial, axis, down)
        shard = jnp.concatenate([before, shard, after], axis=dim)
    return shard


def transpose_conv(padded, weight):
    rows_x = padded.shape[0] - 1
    rows_y = padded.shape[1] - 1
    rows_z = padded.shape[2] - 1
    outputs = weight.shape[4]
    zpair = jnp.concatenate([padded[:, :, :rows_z, :], padded[:, :, 1:, :]], axis=3)
    nothing = jnp.zeros((weight.shape[0], outputs), weight.dtype)
    classes = []
    for parity_x in (0, 1):
        for parity_y in (0, 1):
            pieces = []
            blocks = []
            for tap_x, move_x in parity_taps[parity_x]:
                for tap_y, move_y in parity_taps[parity_y]:
                    pieces.append(zpair[move_x : move_x + rows_x, move_y : move_y + rows_y])
                    taps = weight[:, tap_x, tap_y]
                    first = jnp.concatenate([taps[:, 1], taps[:, 2]], axis=1)
                    second = jnp.concatenate([nothing, taps[:, 0]], axis=1)
                    blocks.append(jnp.concatenate([first, second], axis=0))
            stacked = jnp.concatenate(pieces, axis=3)
            flat = stacked.reshape(-1, stacked.shape[3])
            mixing = jnp.concatenate(blocks, axis=0)
            classes.append(jnp.dot(flat, mixing, preferred_element_type=jnp.float32))
    joined = jnp.stack(classes).reshape(2, 2, rows_x, rows_y, rows_z, 2 * outputs)
    joined = joined.transpose(2, 0, 3, 1, 4, 5)
    return joined.reshape(2 * rows_x, 2 * rows_y, 2 * rows_z, outputs)


def depth_taps(volume):
    count_x, count_y, count_z, channels = volume.shape
    paired = volume.reshape(count_x, count_y, count_z // 2, 2 * channels)
    even = paired[..., :channels]
    odd = paired[..., channels:]
    earlier = jnp.pad(odd[:, :, :-1, :], ((0, 0), (0, 0), (1, 0), (0, 0)))
    return jnp.concatenate([earlier, even, odd], axis=3)


def coarse_terms(hidden, below, gradient):
    count_x, count_y, count_z, filters = gradient.shape
    flat_grad = gradient.reshape(-1, filters)
    stacked = depth_taps(hidden)
    width = stacked.shape[3]
    split = stacked.reshape(count_x, 2, count_y, 2, count_z, width)
    rim = depth_taps(below).reshape(1, count_y, 2, count_z, width)
    by_x = [jnp.concatenate([rim, split[:-1, 1]], axis=0), split[:, 0], split[:, 1]]
    terms = []
    for tap_x in range(3):
        plane = by_x[tap_x]
        by_y = [
            jnp.pad(plane[:, :-1, 1], ((0, 0), (1, 0), (0, 0), (0, 0))),
            plane[:, :, 0],
            plane[:, :, 1],
        ]
        for tap_y in range(3):
            piece = by_y[tap_y].reshape(-1, width)
            terms.append(
                lax.dot_general(
                    flat_grad, piece, (((0,), (0,)), ((), ())), preferred_element_type=jnp.float32
                )
            )
    return jnp.stack(terms, axis=1).reshape(filters, 3, 3, 3, width // 3)


def fine_terms(framed, gradient):
    count_x, count_y, count_z, filters = gradient.shape
    flat_grad = gradient.reshape(-1, filters)
    stacked = jnp.concatenate(
        [framed[:, :, shift : shift + count_z, :] for shift in range(3)], axis=3
    )
    width = stacked.shape[3]
    terms = []
    for tap_x in range(3):
        for tap_y in range(3):
            piece = stacked[tap_x : tap_x + count_x, tap_y : tap_y + count_y].reshape(-1, width)
            terms.append(
                lax.dot_general(
                    flat_grad, piece, (((0,), (0,)), ((), ())), preferred_element_type=jnp.float32
                )
            )
    return jnp.stack(terms, axis=1).reshape(filters, 3, 3, 3, width // 3)


def pair_sum(terms, core, groups):
    halves = terms.reshape(terms.shape[0], 2, -1)
    kept = jnp.where(core == 0, halves[:, 0], halves[:, 1])
    given = jnp.where(core == 0, halves[:, 1], halves[:, 0])
    partner = [(i, i ^ 1) for i in range(groups)]
    return kept + lax.ppermute(given, "dp", partner)


def space_share(whole_terms, parts):
    blocks = whole_terms.reshape((parts, -1) + whole_terms.shape[1:])
    arrived = lax.all_to_all(blocks, "space", split_axis=0, concat_axis=0, tiled=True)
    return arrived.sum(axis=0)


def gathered(block, axis):
    size = lax.axis_size(axis)
    copies = jnp.broadcast_to(block[None], (size,) + block.shape)
    whole = lax.all_to_all(copies, axis, split_axis=0, concat_axis=0, tiled=True)
    return whole.reshape((size * block.shape[0],) + block.shape[1:])


def staged(acts_in, pre_act, weight_two, grad_out):
    parts = lax.axis_size("space")
    groups = lax.axis_size("dp")
    acts = acts_in[0]
    depth, across, height, _ = acts.shape
    scaling = 1.0 / math.sqrt(groups * depth * parts * across * height)
    before_f = pre_act[0].astype(jnp.float32)
    hidden = jnp.where(before_f > 0, before_f, leak_slope * before_f).astype(jnp.bfloat16)
    hidden = lax.optimization_barrier(hidden)
    grad_tile = lax.all_to_all(grad_out, "space", split_axis=1, concat_axis=4, tiled=True)[0]
    below = passed_along(hidden[-1:], "space", 1)
    whole_weight = gathered(weight_two, "space")
    above = passed_along(grad_tile[:1], "space", -1)
    upper = jnp.pad(jnp.concatenate([grad_tile, above], axis=0), ((0, 0), (0, 1), (0, 1), (0, 0)))
    core = lax.axis_index("dp") % 2
    coarse_full = coarse_terms(hidden, below, grad_tile)
    coarse_pair = pair_sum(coarse_full, core, groups)
    coarse_share = space_share(coarse_pair, parts)
    back = transpose_conv(upper, whole_weight)
    delta = (back * jnp.where(hidden > 0, 1.0, leak_slope)).astype(jnp.bfloat16)
    framed = padded_2(acts, (("space", 0),), 1)
    framed = jnp.pad(framed, ((0, 0), (1, 1), (1, 1), (0, 0)))
    fine_full = fine_terms(framed, delta)
    fine_share = space_share(pair_sum(fine_full, core, groups), parts)
    both = jnp.stack([fine_share, coarse_share], axis=0)
    for bit in (2, 4, 8):
        both = both + lax.ppermute(both, "dp", [(i, i ^ bit) for i in range(groups)])
    other = lax.ppermute(both, "dp", [(i, i ^ 1) for i in range(groups)])
    low = jnp.where(core == 0, both, other)
    high = jnp.where(core == 0, other, both)
    total = jnp.concatenate([low, high], axis=2)
    shape = (total.shape[1],) + fine_full.shape[1:]
    return (total[0].reshape(shape) * scaling, total[1].reshape(shape) * scaling)


def solution(mesh):
    placed = (
        P("dp", "space", None, None, None),
        P("dp", "space", None, None, None),
        P("space", None, None, None, None),
        P("dp", None, None, None, "space"),
    )
    return jax.shard_map(
        staged,
        mesh=mesh,
        in_specs=placed,
        out_specs=(P("space", None, None, None, None), P("space", None, None, None, None)),
        check_vma=False,
    )
```

```python
import math

import jax
import jax.numpy as jnp
from jax import lax
from jax.sharding import PartitionSpec as P


leak_slope = 0.3
parity_taps = {0: ((1, 0),), 1: ((0, 1), (2, 0))}


def passed_along(block, axis, distance):
    devices = range(lax.axis_size(axis))
    route = [(i - distance, i) for i in devices if i - distance in devices]
    return lax.ppermute(block, axis, route)


def transpose_conv(padded, weight):
    rows_x = padded.shape[0] - 1
    rows_y = padded.shape[1] - 1
    rows_z = padded.shape[2] - 1
    outputs = weight.shape[4]
    zpair = jnp.concatenate([padded[:, :, :rows_z, :], padded[:, :, 1:, :]], axis=3)
    nothing = jnp.zeros((weight.shape[0], outputs), weight.dtype)
    classes = []
    for parity_x in (0, 1):
        for parity_y in (0, 1):
            pieces = []
            blocks = []
            for tap_x, move_x in parity_taps[parity_x]:
                for tap_y, move_y in parity_taps[parity_y]:
                    pieces.append(zpair[move_x : move_x + rows_x, move_y : move_y + rows_y])
                    taps = weight[:, tap_x, tap_y]
                    first = jnp.concatenate([taps[:, 1], taps[:, 2]], axis=1)
                    second = jnp.concatenate([nothing, taps[:, 0]], axis=1)
                    blocks.append(jnp.concatenate([first, second], axis=0))
            stacked = jnp.concatenate(pieces, axis=3)
            flat = stacked.reshape(-1, stacked.shape[3])
            mixing = jnp.concatenate(blocks, axis=0)
            classes.append(jnp.dot(flat, mixing, preferred_element_type=jnp.float32))
    joined = jnp.stack(classes).reshape(2, 2, rows_x, rows_y, rows_z, 2 * outputs)
    joined = joined.transpose(2, 0, 3, 1, 4, 5)
    return joined.reshape(2 * rows_x, 2 * rows_y, 2 * rows_z, outputs)


def depth_taps(volume):
    count_x, count_y, count_z, channels = volume.shape
    paired = volume.reshape(count_x, count_y, count_z // 2, 2 * channels)
    even = paired[..., :channels]
    odd = paired[..., channels:]
    earlier = jnp.pad(odd[:, :, :-1, :], ((0, 0), (0, 0), (1, 0), (0, 0)))
    return jnp.concatenate([earlier, even, odd], axis=3)


def coarse_terms(hidden, below, gradient):
    count_x, count_y, count_z, filters = gradient.shape
    flat_grad = gradient.reshape(-1, filters)
    stacked = depth_taps(hidden)
    width = stacked.shape[3]
    split = stacked.reshape(count_x, 2, count_y, 2, count_z, width)
    rim = depth_taps(below).reshape(1, count_y, 2, count_z, width)
    by_x = [jnp.concatenate([rim, split[:-1, 1]], axis=0), split[:, 0], split[:, 1]]
    terms = []
    for tap_x in range(3):
        plane = by_x[tap_x]
        by_y = [
            jnp.pad(plane[:, :-1, 1], ((0, 0), (1, 0), (0, 0), (0, 0))),
            plane[:, :, 0],
            plane[:, :, 1],
        ]
        for tap_y in range(3):
            piece = by_y[tap_y].reshape(-1, width)
            terms.append(
                lax.dot_general(
                    flat_grad, piece, (((0,), (0,)), ((), ())), preferred_element_type=jnp.float32
                )
            )
    return jnp.stack(terms, axis=1).reshape(filters, 3, 3, 3, width // 3)


def fine_terms(framed, gradient):
    count_x, count_y, count_z, filters = gradient.shape
    flat_grad = gradient.reshape(-1, filters)
    stacked = jnp.concatenate(
        [framed[:, :, shift : shift + count_z, :] for shift in range(3)], axis=3
    )
    width = stacked.shape[3]
    terms = []
    for tap_x in range(3):
        for tap_y in range(3):
            piece = stacked[tap_x : tap_x + count_x, tap_y : tap_y + count_y].reshape(-1, width)
            terms.append(
                lax.dot_general(
                    flat_grad, piece, (((0,), (0,)), ((), ())), preferred_element_type=jnp.float32
                )
            )
    return jnp.stack(terms, axis=1).reshape(filters, 3, 3, 3, width // 3)


def exchanged(gradient, weight, parts):
    depth, across, height, filters = gradient.shape
    pieces = gradient.reshape(parts, -1)
    copies = jnp.broadcast_to(weight.reshape(1, -1), (parts, weight.size))
    arrived = lax.all_to_all(
        jnp.concatenate([pieces, copies], axis=1), "space", split_axis=0, concat_axis=0, tiled=True
    )
    rows = depth // parts
    tile = arrived[:, : pieces.shape[1]].reshape(parts, rows, across, height, filters)
    tile = tile.transpose(1, 2, 3, 0, 4).reshape(rows, across, height, parts * filters)
    whole = arrived[:, pieces.shape[1] :].reshape((parts * weight.shape[0],) + weight.shape[1:])
    return tile, whole


def pair_sum(terms, core, groups):
    halves = terms.reshape(terms.shape[0], 2, -1)
    kept = jnp.where(core == 0, halves[:, 0], halves[:, 1])
    given = jnp.where(core == 0, halves[:, 1], halves[:, 0])
    partner = [(i, i ^ 1) for i in range(groups)]
    return kept + lax.ppermute(given, "dp", partner)


def space_share(whole_terms, parts):
    blocks = whole_terms.reshape((parts, -1) + whole_terms.shape[1:])
    arrived = lax.all_to_all(blocks, "space", split_axis=0, concat_axis=0, tiled=True)
    return arrived.sum(axis=0)


def staged(acts_in, pre_act, weight_two, grad_out):
    parts = lax.axis_size("space")
    groups = lax.axis_size("dp")
    acts = acts_in[0]
    depth, across, height, channels = acts.shape
    scaling = 1.0 / math.sqrt(groups * depth * parts * across * height)
    before_f = pre_act[0].astype(jnp.float32)
    hidden = jnp.where(before_f > 0, before_f, leak_slope * before_f).astype(jnp.bfloat16)
    hidden = lax.optimization_barrier(hidden)
    grad_tile, whole_weight = exchanged(grad_out[0], weight_two, parts)
    sent_up = jnp.stack([acts[-1], hidden[-1]])
    from_below = passed_along(sent_up, "space", 1)
    before, below = from_below[:1], from_below[1:]
    plane = acts[0].reshape(-1, channels)
    sent_down = jnp.concatenate([plane, grad_tile[0].reshape(-1, channels)], axis=0)
    from_above = passed_along(sent_down, "space", -1)
    after = from_above[: plane.shape[0]].reshape((1,) + acts.shape[1:])
    above = from_above[plane.shape[0] :].reshape((1,) + grad_tile.shape[1:])
    upper = jnp.pad(jnp.concatenate([grad_tile, above], axis=0), ((0, 0), (0, 1), (0, 1), (0, 0)))
    core = lax.axis_index("dp") % 2
    coarse_full = coarse_terms(hidden, below, grad_tile)
    coarse_pair = pair_sum(coarse_full, core, groups)
    coarse_share = space_share(coarse_pair, parts)
    back = transpose_conv(upper, whole_weight)
    delta = (back * jnp.where(hidden > 0, 1.0, leak_slope)).astype(jnp.bfloat16)
    framed = jnp.concatenate([before, acts, after], axis=0)
    framed = jnp.pad(framed, ((0, 0), (1, 1), (1, 1), (0, 0)))
    fine_full = fine_terms(framed, delta)
    fine_share = space_share(pair_sum(fine_full, core, groups), parts)
    both = jnp.stack([fine_share, coarse_share], axis=0)
    for bit in (2, 4, 8):
        both = both + lax.ppermute(both, "dp", [(i, i ^ bit) for i in range(groups)])
    other = lax.ppermute(both, "dp", [(i, i ^ 1) for i in range(groups)])
    low = jnp.where(core == 0, both, other)
    high = jnp.where(core == 0, other, both)
    total = jnp.concatenate([low, high], axis=2)
    shape = (total.shape[1],) + fine_full.shape[1:]
    return (total[0].reshape(shape) * scaling, total[1].reshape(shape) * scaling)


def solution(mesh):
    placed = (
        P("dp", "space", None, None, None),
        P("dp", "space", None, None, None),
        P("space", None, None, None, None),
        P("dp", None, None, None, "space"),
    )
    return jax.shard_map(
        staged,
        mesh=mesh,
        in_specs=placed,
        out_specs=(P("space", None, None, None, None), P("space", None, None, None, None)),
        check_vma=False,
    )
```

```python
import math

import jax
import jax.numpy as jnp
from jax import lax
from jax.sharding import PartitionSpec as P


leak_slope = 0.3
parity_taps = {0: ((1, 0),), 1: ((0, 1), (2, 0))}


def passed_along(block, axis, distance):
    devices = range(lax.axis_size(axis))
    route = [(i - distance, i) for i in devices if i - distance in devices]
    return lax.ppermute(block, axis, route)


def padded_2(shard, sides, width):
    for axis, dim in sides:
        size, length = (lax.axis_size(axis), shard.shape[dim])
        up = [(i, (i + 1) % size) for i in range(size - 1)]
        down = [(j, i) for i, j in up]
        last = lax.slice_in_dim(shard, length - width, length, axis=dim)
        initial = lax.slice_in_dim(shard, 0, width, axis=dim)
        before = lax.ppermute(last, axis, up)
        after = lax.ppermute(initial, axis, down)
        shard = jnp.concatenate([before, shard, after], axis=dim)
    return shard


def transpose_conv(padded, weight):
    rows_x = padded.shape[0] - 1
    rows_y = padded.shape[1] - 1
    rows_z = padded.shape[2] - 1
    outputs = weight.shape[4]
    zpair = jnp.concatenate([padded[:, :, :rows_z, :], padded[:, :, 1:, :]], axis=3)
    nothing = jnp.zeros((weight.shape[0], outputs), weight.dtype)
    classes = []
    for parity_x in (0, 1):
        for parity_y in (0, 1):
            pieces = []
            blocks = []
            for tap_x, move_x in parity_taps[parity_x]:
                for tap_y, move_y in parity_taps[parity_y]:
                    pieces.append(zpair[move_x : move_x + rows_x, move_y : move_y + rows_y])
                    taps = weight[:, tap_x, tap_y]
                    first = jnp.concatenate([taps[:, 1], taps[:, 2]], axis=1)
                    second = jnp.concatenate([nothing, taps[:, 0]], axis=1)
                    blocks.append(jnp.concatenate([first, second], axis=0))
            stacked = jnp.concatenate(pieces, axis=3)
            flat = stacked.reshape(-1, stacked.shape[3])
            mixing = jnp.concatenate(blocks, axis=0)
            classes.append(jnp.dot(flat, mixing, preferred_element_type=jnp.float32))
    joined = jnp.stack(classes).reshape(2, 2, rows_x, rows_y, rows_z, 2 * outputs)
    joined = joined.transpose(2, 0, 3, 1, 4, 5)
    return joined.reshape(2 * rows_x, 2 * rows_y, 2 * rows_z, outputs)


def depth_taps(volume):
    count_x, count_y, count_z, channels = volume.shape
    paired = volume.reshape(count_x, count_y, count_z // 2, 2 * channels)
    even = paired[..., :channels]
    odd = paired[..., channels:]
    earlier = jnp.pad(odd[:, :, :-1, :], ((0, 0), (0, 0), (1, 0), (0, 0)))
    return jnp.concatenate([earlier, even, odd], axis=3)


def coarse_terms(hidden, below, gradient):
    count_x, count_y, count_z, filters = gradient.shape
    flat_grad = gradient.reshape(-1, filters)
    stacked = depth_taps(hidden)
    width = stacked.shape[3]
    split = stacked.reshape(count_x, 2, count_y, 2, count_z, width)
    rim = depth_taps(below).reshape(1, count_y, 2, count_z, width)
    by_x = [jnp.concatenate([rim, split[:-1, 1]], axis=0), split[:, 0], split[:, 1]]
    terms = []
    for tap_x in range(3):
        plane = by_x[tap_x]
        by_y = [
            jnp.pad(plane[:, :-1, 1], ((0, 0), (1, 0), (0, 0), (0, 0))),
            plane[:, :, 0],
            plane[:, :, 1],
        ]
        for tap_y in range(3):
            piece = by_y[tap_y].reshape(-1, width)
            terms.append(
                lax.dot_general(
                    flat_grad, piece, (((0,), (0,)), ((), ())), preferred_element_type=jnp.float32
                )
            )
    return jnp.stack(terms, axis=1).reshape(filters, 3, 3, 3, width // 3)


def fine_stacked(framed, gradient):
    count_x, count_y, count_z, filters = gradient.shape
    channels = framed.shape[3]
    padded = jnp.pad(gradient, ((0, 0), (2, 2), (0, 0), (0, 0)))
    shifted = jnp.concatenate(
        [padded[:, 2 - tap_y : 4 - tap_y + count_y] for tap_y in range(3)], axis=3
    )
    flat_grad = shifted.reshape(-1, shifted.shape[3])
    terms = []
    for tap_x in range(3):
        for tap_z in range(3):
            window = framed[tap_x : tap_x + count_x, :, tap_z : tap_z + count_z, :]
            terms.append(
                lax.dot_general(
                    flat_grad,
                    window.reshape(-1, channels),
                    (((0,), (0,)), ((), ())),
                    preferred_element_type=jnp.float32,
                )
            )
    joined = jnp.stack(terms).reshape(3, 3, 3, filters, channels)
    return joined.transpose(3, 0, 2, 1, 4)


def rows_with_next(gradient, parts):
    count = gradient.shape[1]
    rows = count // parts
    rest = gradient.shape[2:]
    grown = jnp.pad(gradient, ((0, 0), (0, rows), (0, 0), (0, 0), (0, 0)))
    own = gradient.reshape((1, parts, rows) + rest)
    following = grown[:, rows : count + rows : rows].reshape((1, parts, 1) + rest)
    sent = jnp.concatenate([own, following], axis=2).reshape((1, parts * (rows + 1)) + rest)
    return lax.all_to_all(sent, "space", split_axis=1, concat_axis=4, tiled=True)[0]


def pair_sum(terms, core, groups):
    halves = terms.reshape(terms.shape[0], 2, -1)
    kept = jnp.where(core == 0, halves[:, 0], halves[:, 1])
    given = jnp.where(core == 0, halves[:, 1], halves[:, 0])
    partner = [(i, i ^ 1) for i in range(groups)]
    return kept + lax.ppermute(given, "dp", partner)


def space_share(whole_terms, parts):
    blocks = whole_terms.reshape((parts, -1) + whole_terms.shape[1:])
    arrived = lax.all_to_all(blocks, "space", split_axis=0, concat_axis=0, tiled=True)
    return arrived.sum(axis=0)


def gathered(block, axis):
    size = lax.axis_size(axis)
    copies = jnp.broadcast_to(block[None], (size,) + block.shape)
    whole = lax.all_to_all(copies, axis, split_axis=0, concat_axis=0, tiled=True)
    return whole.reshape((size * block.shape[0],) + block.shape[1:])


def staged(acts_in, pre_act, weight_two, grad_out):
    parts = lax.axis_size("space")
    groups = lax.axis_size("dp")
    acts = acts_in[0]
    depth, across, height, _ = acts.shape
    scaling = 1.0 / math.sqrt(groups * depth * parts * across * height)
    before_f = pre_act[0].astype(jnp.float32)
    hidden = jnp.where(before_f > 0, before_f, leak_slope * before_f).astype(jnp.bfloat16)
    hidden = lax.optimization_barrier(hidden)
    upper = rows_with_next(grad_out, parts)
    grad_tile = upper[:-1]
    below = passed_along(hidden[-1:], "space", 1)
    whole_weight = gathered(weight_two, "space")
    upper = jnp.pad(upper, ((0, 0), (0, 1), (0, 1), (0, 0)))
    core = lax.axis_index("dp") % 2
    coarse_full = coarse_terms(hidden, below, grad_tile)
    coarse_pair = pair_sum(coarse_full, core, groups)
    coarse_share = space_share(coarse_pair, parts)
    back = transpose_conv(upper, whole_weight)
    delta = (back * jnp.where(hidden > 0, 1.0, leak_slope)).astype(jnp.bfloat16)
    framed = padded_2(acts, (("space", 0),), 1)
    framed = jnp.pad(framed, ((0, 0), (1, 1), (1, 1), (0, 0)))
    fine_full = fine_stacked(framed, delta)
    fine_share = space_share(pair_sum(fine_full, core, groups), parts)
    both = jnp.stack([fine_share, coarse_share], axis=0)
    for bit in (2, 4, 8):
        both = both + lax.ppermute(both, "dp", [(i, i ^ bit) for i in range(groups)])
    other = lax.ppermute(both, "dp", [(i, i ^ 1) for i in range(groups)])
    low = jnp.where(core == 0, both, other)
    high = jnp.where(core == 0, other, both)
    total = jnp.concatenate([low, high], axis=2)
    shape = (total.shape[1],) + fine_full.shape[1:]
    return (total[0].reshape(shape) * scaling, total[1].reshape(shape) * scaling)


def solution(mesh):
    placed = (
        P("dp", "space", None, None, None),
        P("dp", "space", None, None, None),
        P("space", None, None, None, None),
        P("dp", None, None, None, "space"),
    )
    return jax.shard_map(
        staged,
        mesh=mesh,
        in_specs=placed,
        out_specs=(P("space", None, None, None, None), P("space", None, None, None, None)),
        check_vma=False,
    )
```

```python
import math

import jax
import jax.numpy as jnp
from jax import lax
from jax.sharding import PartitionSpec as P


leak_slope = 0.3
parity_taps = {0: ((1, 0),), 1: ((0, 1), (2, 0))}


def passed_along(block, axis, distance):
    devices = range(lax.axis_size(axis))
    route = [(i - distance, i) for i in devices if i - distance in devices]
    return lax.ppermute(block, axis, route)


def padded_2(shard, sides, width):
    for axis, dim in sides:
        size, length = (lax.axis_size(axis), shard.shape[dim])
        up = [(i, (i + 1) % size) for i in range(size - 1)]
        down = [(j, i) for i, j in up]
        last = lax.slice_in_dim(shard, length - width, length, axis=dim)
        initial = lax.slice_in_dim(shard, 0, width, axis=dim)
        before = lax.ppermute(last, axis, up)
        after = lax.ppermute(initial, axis, down)
        shard = jnp.concatenate([before, shard, after], axis=dim)
    return shard


def transpose_conv(padded, weight):
    rows_x = padded.shape[0] - 1
    rows_y = padded.shape[1] - 1
    rows_z = padded.shape[2] - 1
    outputs = weight.shape[4]
    zpair = jnp.concatenate([padded[:, :, :rows_z, :], padded[:, :, 1:, :]], axis=3)
    nothing = jnp.zeros((weight.shape[0], outputs), weight.dtype)
    classes = []
    for parity_x in (0, 1):
        for parity_y in (0, 1):
            pieces = []
            blocks = []
            for tap_x, move_x in parity_taps[parity_x]:
                for tap_y, move_y in parity_taps[parity_y]:
                    pieces.append(zpair[move_x : move_x + rows_x, move_y : move_y + rows_y])
                    taps = weight[:, tap_x, tap_y]
                    first = jnp.concatenate([taps[:, 1], taps[:, 2]], axis=1)
                    second = jnp.concatenate([nothing, taps[:, 0]], axis=1)
                    blocks.append(jnp.concatenate([first, second], axis=0))
            stacked = jnp.concatenate(pieces, axis=3)
            flat = stacked.reshape(-1, stacked.shape[3])
            mixing = jnp.concatenate(blocks, axis=0)
            classes.append(jnp.dot(flat, mixing, preferred_element_type=jnp.float32))
    joined = jnp.stack(classes).reshape(2, 2, rows_x, rows_y, rows_z, 2 * outputs)
    joined = joined.transpose(2, 0, 3, 1, 4, 5)
    return joined.reshape(2 * rows_x, 2 * rows_y, 2 * rows_z, outputs)


def depth_taps(volume):
    count_x, count_y, count_z, channels = volume.shape
    paired = volume.reshape(count_x, count_y, count_z // 2, 2 * channels)
    even = paired[..., :channels]
    odd = paired[..., channels:]
    earlier = jnp.pad(odd[:, :, :-1, :], ((0, 0), (0, 0), (1, 0), (0, 0)))
    return jnp.concatenate([earlier, even, odd], axis=3)


def coarse_terms(hidden, below, gradient):
    count_x, count_y, count_z, filters = gradient.shape
    flat_grad = gradient.reshape(-1, filters)
    stacked = depth_taps(hidden)
    width = stacked.shape[3]
    split = stacked.reshape(count_x, 2, count_y, 2, count_z, width)
    rim = depth_taps(below).reshape(1, count_y, 2, count_z, width)
    by_x = [jnp.concatenate([rim, split[:-1, 1]], axis=0), split[:, 0], split[:, 1]]
    terms = []
    for tap_x in range(3):
        plane = by_x[tap_x]
        by_y = [
            jnp.pad(plane[:, :-1, 1], ((0, 0), (1, 0), (0, 0), (0, 0))),
            plane[:, :, 0],
            plane[:, :, 1],
        ]
        for tap_y in range(3):
            piece = by_y[tap_y].reshape(-1, width)
            terms.append(
                lax.dot_general(
                    flat_grad, piece, (((0,), (0,)), ((), ())), preferred_element_type=jnp.float32
                )
            )
    return jnp.stack(terms, axis=1).reshape(filters, 3, 3, 3, width // 3)


def fine_stacked(framed, gradient):
    count_x, count_y, count_z, filters = gradient.shape
    channels = framed.shape[3]
    padded = jnp.pad(gradient, ((0, 0), (2, 2), (0, 0), (0, 0)))
    shifted = jnp.concatenate(
        [padded[:, 2 - tap_y : 4 - tap_y + count_y] for tap_y in range(3)], axis=3
    )
    flat_grad = shifted.reshape(-1, shifted.shape[3])
    terms = []
    for tap_x in range(3):
        for tap_z in range(3):
            window = framed[tap_x : tap_x + count_x, :, tap_z : tap_z + count_z, :]
            terms.append(
                lax.dot_general(
                    flat_grad,
                    window.reshape(-1, channels),
                    (((0,), (0,)), ((), ())),
                    preferred_element_type=jnp.float32,
                )
            )
    joined = jnp.stack(terms).reshape(3, 3, 3, filters, channels)
    return joined.transpose(3, 0, 2, 1, 4)


def same_core_total(share, groups):
    place = lax.axis_index("dp") // 2
    held = [share] + [
        lax.ppermute(share, "dp", [(i, i ^ (2 * step)) for i in range(groups)])
        for step in range(1, groups // 2)
    ]
    held = jnp.stack(held)
    ordered = jnp.take(held, place ^ jnp.arange(groups // 2), axis=0)
    total = ordered[0]
    for step in range(1, groups // 2):
        total = total + ordered[step]
    return total


def pair_sum(terms, core, groups):
    halves = terms.reshape(terms.shape[0], 2, -1)
    kept = jnp.where(core == 0, halves[:, 0], halves[:, 1])
    given = jnp.where(core == 0, halves[:, 1], halves[:, 0])
    partner = [(i, i ^ 1) for i in range(groups)]
    return kept + lax.ppermute(given, "dp", partner)


def space_share(whole_terms, parts):
    blocks = whole_terms.reshape((parts, -1) + whole_terms.shape[1:])
    arrived = lax.all_to_all(blocks, "space", split_axis=0, concat_axis=0, tiled=True)
    return arrived.sum(axis=0)


def gathered(block, axis):
    size = lax.axis_size(axis)
    copies = jnp.broadcast_to(block[None], (size,) + block.shape)
    whole = lax.all_to_all(copies, axis, split_axis=0, concat_axis=0, tiled=True)
    return whole.reshape((size * block.shape[0],) + block.shape[1:])


def staged(acts_in, pre_act, weight_two, grad_out):
    parts = lax.axis_size("space")
    groups = lax.axis_size("dp")
    acts = acts_in[0]
    depth, across, height, _ = acts.shape
    scaling = 1.0 / math.sqrt(groups * depth * parts * across * height)
    before_f = pre_act[0].astype(jnp.float32)
    hidden = jnp.where(before_f > 0, before_f, leak_slope * before_f).astype(jnp.bfloat16)
    hidden = lax.optimization_barrier(hidden)
    grad_tile = lax.all_to_all(grad_out, "space", split_axis=1, concat_axis=4, tiled=True)[0]
    below = passed_along(hidden[-1:], "space", 1)
    whole_weight = gathered(weight_two, "space")
    above = passed_along(grad_tile[:1], "space", -1)
    upper = jnp.pad(jnp.concatenate([grad_tile, above], axis=0), ((0, 0), (0, 1), (0, 1), (0, 0)))
    core = lax.axis_index("dp") % 2
    coarse_full = coarse_terms(hidden, below, grad_tile)
    coarse_pair = pair_sum(coarse_full, core, groups)
    coarse_share = space_share(coarse_pair, parts)
    back = transpose_conv(upper, whole_weight)
    delta = (back * jnp.where(hidden > 0, 1.0, leak_slope)).astype(jnp.bfloat16)
    framed = padded_2(acts, (("space", 0),), 1)
    framed = jnp.pad(framed, ((0, 0), (1, 1), (1, 1), (0, 0)))
    fine_full = fine_stacked(framed, delta)
    fine_share = space_share(pair_sum(fine_full, core, groups), parts)
    both = jnp.stack([fine_share, coarse_share], axis=0)
    both = same_core_total(both, groups)
    other = lax.ppermute(both, "dp", [(i, i ^ 1) for i in range(groups)])
    low = jnp.where(core == 0, both, other)
    high = jnp.where(core == 0, other, both)
    total = jnp.concatenate([low, high], axis=2)
    shape = (total.shape[1],) + fine_full.shape[1:]
    return (total[0].reshape(shape) * scaling, total[1].reshape(shape) * scaling)


def solution(mesh):
    placed = (
        P("dp", "space", None, None, None),
        P("dp", "space", None, None, None),
        P("space", None, None, None, None),
        P("dp", None, None, None, "space"),
    )
    return jax.shard_map(
        staged,
        mesh=mesh,
        in_specs=placed,
        out_specs=(P("space", None, None, None, None), P("space", None, None, None, None)),
        check_vma=False,
    )
```

```python
import math

import jax
import jax.numpy as jnp
from jax import lax
from jax.sharding import PartitionSpec as P


leak_slope = 0.3
parity_taps = {0: ((1, 0),), 1: ((0, 1), (2, 0))}


def passed_along(block, axis, distance):
    devices = range(lax.axis_size(axis))
    route = [(i - distance, i) for i in devices if i - distance in devices]
    return lax.ppermute(block, axis, route)


def padded_2(shard, sides, width):
    for axis, dim in sides:
        size, length = (lax.axis_size(axis), shard.shape[dim])
        up = [(i, (i + 1) % size) for i in range(size - 1)]
        down = [(j, i) for i, j in up]
        last = lax.slice_in_dim(shard, length - width, length, axis=dim)
        initial = lax.slice_in_dim(shard, 0, width, axis=dim)
        before = lax.ppermute(last, axis, up)
        after = lax.ppermute(initial, axis, down)
        shard = jnp.concatenate([before, shard, after], axis=dim)
    return shard


def transpose_delta(padded, weight, hidden):
    rows_x = padded.shape[0] - 1
    rows_y = padded.shape[1] - 1
    rows_z = padded.shape[2] - 1
    outputs = weight.shape[4]
    zpair = jnp.concatenate([padded[:, :, :rows_z, :], padded[:, :, 1:, :]], axis=3)
    nothing = jnp.zeros((weight.shape[0], outputs), weight.dtype)
    classes = []
    for parity_x in (0, 1):
        for parity_y in (0, 1):
            pieces = []
            blocks = []
            for tap_x, move_x in parity_taps[parity_x]:
                for tap_y, move_y in parity_taps[parity_y]:
                    pieces.append(zpair[move_x : move_x + rows_x, move_y : move_y + rows_y])
                    taps = weight[:, tap_x, tap_y]
                    first = jnp.concatenate([taps[:, 1], taps[:, 2]], axis=1)
                    second = jnp.concatenate([nothing, taps[:, 0]], axis=1)
                    blocks.append(jnp.concatenate([first, second], axis=0))
            stacked = jnp.concatenate(pieces, axis=3)
            flat = stacked.reshape(-1, stacked.shape[3])
            mixing = jnp.concatenate(blocks, axis=0)
            classes.append(jnp.dot(flat, mixing, preferred_element_type=jnp.float32))
    joined = jnp.stack(classes).reshape(2, 2, rows_x, rows_y, rows_z, 2 * outputs)
    sign = hidden.reshape(rows_x, 2, rows_y, 2, rows_z, 2 * outputs).transpose(1, 3, 0, 2, 4, 5)
    small = (joined * jnp.where(sign > 0, 1.0, leak_slope)).astype(jnp.bfloat16)
    small = small.transpose(2, 0, 3, 1, 4, 5)
    return small.reshape(2 * rows_x, 2 * rows_y, 2 * rows_z, outputs)


def depth_taps(volume):
    count_x, count_y, count_z, channels = volume.shape
    paired = volume.reshape(count_x, count_y, count_z // 2, 2 * channels)
    even = paired[..., :channels]
    odd = paired[..., channels:]
    earlier = jnp.pad(odd[:, :, :-1, :], ((0, 0), (0, 0), (1, 0), (0, 0)))
    return jnp.concatenate([earlier, even, odd], axis=3)


def coarse_terms(hidden, below, gradient):
    count_x, count_y, count_z, filters = gradient.shape
    flat_grad = gradient.reshape(-1, filters)
    stacked = depth_taps(hidden)
    width = stacked.shape[3]
    split = stacked.reshape(count_x, 2, count_y, 2, count_z, width)
    rim = depth_taps(below).reshape(1, count_y, 2, count_z, width)
    by_x = [jnp.concatenate([rim, split[:-1, 1]], axis=0), split[:, 0], split[:, 1]]
    terms = []
    for tap_x in range(3):
        plane = by_x[tap_x]
        by_y = [
            jnp.pad(plane[:, :-1, 1], ((0, 0), (1, 0), (0, 0), (0, 0))),
            plane[:, :, 0],
            plane[:, :, 1],
        ]
        for tap_y in range(3):
            piece = by_y[tap_y].reshape(-1, width)
            terms.append(
                lax.dot_general(
                    flat_grad, piece, (((0,), (0,)), ((), ())), preferred_element_type=jnp.float32
                )
            )
    return jnp.stack(terms, axis=1).reshape(filters, 3, 3, 3, width // 3)


def fine_stacked(framed, gradient):
    count_x, count_y, count_z, filters = gradient.shape
    channels = framed.shape[3]
    padded = jnp.pad(gradient, ((0, 0), (2, 2), (0, 0), (0, 0)))
    shifted = jnp.concatenate(
        [padded[:, 2 - tap_y : 4 - tap_y + count_y] for tap_y in range(3)], axis=3
    )
    flat_grad = shifted.reshape(-1, shifted.shape[3])
    terms = []
    for tap_x in range(3):
        for tap_z in range(3):
            window = framed[tap_x : tap_x + count_x, :, tap_z : tap_z + count_z, :]
            terms.append(
                lax.dot_general(
                    flat_grad,
                    window.reshape(-1, channels),
                    (((0,), (0,)), ((), ())),
                    preferred_element_type=jnp.float32,
                )
            )
    joined = jnp.stack(terms).reshape(3, 3, 3, filters, channels)
    return joined.transpose(3, 0, 2, 1, 4)


def pair_sum(terms, core, groups):
    halves = terms.reshape(terms.shape[0], 2, -1)
    kept = jnp.where(core == 0, halves[:, 0], halves[:, 1])
    given = jnp.where(core == 0, halves[:, 1], halves[:, 0])
    partner = [(i, i ^ 1) for i in range(groups)]
    return kept + lax.ppermute(given, "dp", partner)


def space_share(whole_terms, parts):
    blocks = whole_terms.reshape((parts, -1) + whole_terms.shape[1:])
    arrived = lax.all_to_all(blocks, "space", split_axis=0, concat_axis=0, tiled=True)
    return arrived.sum(axis=0)


def gathered(block, axis):
    size = lax.axis_size(axis)
    copies = jnp.broadcast_to(block[None], (size,) + block.shape)
    whole = lax.all_to_all(copies, axis, split_axis=0, concat_axis=0, tiled=True)
    return whole.reshape((size * block.shape[0],) + block.shape[1:])


def staged(acts_in, pre_act, weight_two, grad_out):
    parts = lax.axis_size("space")
    groups = lax.axis_size("dp")
    acts = acts_in[0]
    depth, across, height, _ = acts.shape
    scaling = 1.0 / math.sqrt(groups * depth * parts * across * height)
    before_f = pre_act[0].astype(jnp.float32)
    hidden = jnp.where(before_f > 0, before_f, leak_slope * before_f).astype(jnp.bfloat16)
    hidden = lax.optimization_barrier(hidden)
    grad_tile = lax.all_to_all(grad_out, "space", split_axis=1, concat_axis=4, tiled=True)[0]
    below = passed_along(hidden[-1:], "space", 1)
    whole_weight = gathered(weight_two, "space")
    above = passed_along(grad_tile[:1], "space", -1)
    upper = jnp.pad(jnp.concatenate([grad_tile, above], axis=0), ((0, 0), (0, 1), (0, 1), (0, 0)))
    core = lax.axis_index("dp") % 2
    coarse_full = coarse_terms(hidden, below, grad_tile)
    coarse_pair = pair_sum(coarse_full, core, groups)
    coarse_share = space_share(coarse_pair, parts)
    delta = transpose_delta(upper, whole_weight, hidden)
    framed = padded_2(acts, (("space", 0),), 1)
    framed = jnp.pad(framed, ((0, 0), (1, 1), (1, 1), (0, 0)))
    fine_full = fine_stacked(framed, delta)
    fine_share = space_share(pair_sum(fine_full, core, groups), parts)
    both = jnp.stack([fine_share, coarse_share], axis=0)
    for bit in (2, 4, 8):
        both = both + lax.ppermute(both, "dp", [(i, i ^ bit) for i in range(groups)])
    other = lax.ppermute(both, "dp", [(i, i ^ 1) for i in range(groups)])
    low = jnp.where(core == 0, both, other)
    high = jnp.where(core == 0, other, both)
    total = jnp.concatenate([low, high], axis=2)
    shape = (total.shape[1],) + fine_full.shape[1:]
    return (total[0].reshape(shape) * scaling, total[1].reshape(shape) * scaling)


def solution(mesh):
    placed = (
        P("dp", "space", None, None, None),
        P("dp", "space", None, None, None),
        P("space", None, None, None, None),
        P("dp", None, None, None, "space"),
    )
    return jax.shard_map(
        staged,
        mesh=mesh,
        in_specs=placed,
        out_specs=(P("space", None, None, None, None), P("space", None, None, None, None)),
        check_vma=False,
    )
```

```python
import math

import jax
import jax.numpy as jnp
from jax import lax
from jax.sharding import PartitionSpec as P


leak_slope = 0.3
parity_taps = {0: ((1, 0),), 1: ((0, 1), (2, 0))}


def passed_along(block, axis, distance):
    devices = range(lax.axis_size(axis))
    route = [(i - distance, i) for i in devices if i - distance in devices]
    return lax.ppermute(block, axis, route)


def padded_2(shard, sides, width):
    for axis, dim in sides:
        size, length = (lax.axis_size(axis), shard.shape[dim])
        up = [(i, (i + 1) % size) for i in range(size - 1)]
        down = [(j, i) for i, j in up]
        last = lax.slice_in_dim(shard, length - width, length, axis=dim)
        initial = lax.slice_in_dim(shard, 0, width, axis=dim)
        before = lax.ppermute(last, axis, up)
        after = lax.ppermute(initial, axis, down)
        shard = jnp.concatenate([before, shard, after], axis=dim)
    return shard


def transpose_conv(padded, weight):
    rows_x = padded.shape[0] - 1
    rows_y = padded.shape[1] - 1
    rows_z = padded.shape[2] - 1
    outputs = weight.shape[4]
    zpair = jnp.concatenate([padded[:, :, :rows_z, :], padded[:, :, 1:, :]], axis=3)
    nothing = jnp.zeros((weight.shape[0], outputs), weight.dtype)
    classes = []
    for parity_x in (0, 1):
        for parity_y in (0, 1):
            pieces = []
            blocks = []
            for tap_x, move_x in parity_taps[parity_x]:
                for tap_y, move_y in parity_taps[parity_y]:
                    pieces.append(zpair[move_x : move_x + rows_x, move_y : move_y + rows_y])
                    taps = weight[:, tap_x, tap_y]
                    first = jnp.concatenate([taps[:, 1], taps[:, 2]], axis=1)
                    second = jnp.concatenate([nothing, taps[:, 0]], axis=1)
                    blocks.append(jnp.concatenate([first, second], axis=0))
            stacked = jnp.concatenate(pieces, axis=3)
            flat = stacked.reshape(-1, stacked.shape[3])
            mixing = jnp.concatenate(blocks, axis=0)
            classes.append(jnp.dot(flat, mixing, preferred_element_type=jnp.float32))
    joined = jnp.stack(classes).reshape(2, 2, rows_x, rows_y, rows_z, 2 * outputs)
    joined = joined.transpose(2, 0, 3, 1, 4, 5)
    return joined.reshape(2 * rows_x, 2 * rows_y, 2 * rows_z, outputs)


def depth_taps(volume):
    count_x, count_y, count_z, channels = volume.shape
    paired = volume.reshape(count_x, count_y, count_z // 2, 2 * channels)
    even = paired[..., :channels]
    odd = paired[..., channels:]
    earlier = jnp.pad(odd[:, :, :-1, :], ((0, 0), (0, 0), (1, 0), (0, 0)))
    return jnp.concatenate([earlier, even, odd], axis=3)


def coarse_terms(hidden, below, gradient):
    count_x, count_y, count_z, filters = gradient.shape
    flat_grad = gradient.reshape(-1, filters)
    stacked = depth_taps(hidden)
    width = stacked.shape[3]
    split = stacked.reshape(count_x, 2, count_y, 2, count_z, width)
    rim = depth_taps(below).reshape(1, count_y, 2, count_z, width)
    by_x = [jnp.concatenate([rim, split[:-1, 1]], axis=0), split[:, 0], split[:, 1]]
    terms = []
    for tap_x in range(3):
        plane = by_x[tap_x]
        by_y = [
            jnp.pad(plane[:, :-1, 1], ((0, 0), (1, 0), (0, 0), (0, 0))),
            plane[:, :, 0],
            plane[:, :, 1],
        ]
        for tap_y in range(3):
            piece = by_y[tap_y].reshape(-1, width)
            terms.append(
                lax.dot_general(
                    flat_grad, piece, (((0,), (0,)), ((), ())), preferred_element_type=jnp.float32
                )
            )
    return jnp.stack(terms, axis=1).reshape(filters, 3, 3, 3, width // 3)


def fine_stacked(framed, gradient):
    count_x, count_y, count_z, filters = gradient.shape
    channels = framed.shape[3]
    padded = jnp.pad(gradient, ((0, 0), (2, 2), (0, 0), (0, 0)))
    shifted = jnp.concatenate(
        [padded[:, 2 - tap_y : 4 - tap_y + count_y] for tap_y in range(3)], axis=3
    )
    flat_grad = shifted.reshape(-1, shifted.shape[3])
    terms = []
    for tap_x in range(3):
        for tap_z in range(3):
            window = framed[tap_x : tap_x + count_x, :, tap_z : tap_z + count_z, :]
            terms.append(
                lax.dot_general(
                    flat_grad,
                    window.reshape(-1, channels),
                    (((0,), (0,)), ((), ())),
                    preferred_element_type=jnp.float32,
                )
            )
    joined = jnp.stack(terms).reshape(3, 3, 3, filters, channels)
    return joined.transpose(3, 0, 2, 1, 4)


def pair_sum(terms, core, groups):
    halves = terms.reshape(terms.shape[0], 2, -1)
    kept = jnp.where(core == 0, halves[:, 0], halves[:, 1])
    given = jnp.where(core == 0, halves[:, 1], halves[:, 0])
    partner = [(i, i ^ 1) for i in range(groups)]
    return kept + lax.ppermute(given, "dp", partner)


def space_share(whole_terms, parts):
    blocks = whole_terms.reshape((parts, -1) + whole_terms.shape[1:])
    arrived = lax.all_to_all(blocks, "space", split_axis=0, concat_axis=0, tiled=True)
    return arrived.sum(axis=0)


def gathered(block, axis):
    size = lax.axis_size(axis)
    copies = jnp.broadcast_to(block[None], (size,) + block.shape)
    whole = lax.all_to_all(copies, axis, split_axis=0, concat_axis=0, tiled=True)
    return whole.reshape((size * block.shape[0],) + block.shape[1:])


def staged(acts_in, pre_act, weight_two, grad_out):
    parts = lax.axis_size("space")
    groups = lax.axis_size("dp")
    acts = acts_in[0]
    depth, across, height, _ = acts.shape
    scaling = 1.0 / math.sqrt(groups * depth * parts * across * height)
    before_f = pre_act[0].astype(jnp.float32)
    hidden = jnp.where(before_f > 0, before_f, leak_slope * before_f).astype(jnp.bfloat16)
    hidden = lax.optimization_barrier(hidden)
    grad_tile = lax.all_to_all(grad_out, "space", split_axis=1, concat_axis=4, tiled=True)[0]
    below = passed_along(hidden[-1:], "space", 1)
    whole_weight = gathered(weight_two, "space")
    above = passed_along(grad_tile[:1], "space", -1)
    upper = jnp.pad(jnp.concatenate([grad_tile, above], axis=0), ((0, 0), (0, 1), (0, 1), (0, 0)))
    core = lax.axis_index("dp") % 2
    coarse_full = coarse_terms(hidden, below, grad_tile)
    coarse_pair = pair_sum(coarse_full, core, groups)
    coarse_share = space_share(coarse_pair, parts)
    back = transpose_conv(upper, whole_weight)
    delta = (back * jnp.where(hidden > 0, 1.0, leak_slope)).astype(jnp.bfloat16)
    framed = padded_2(acts, (("space", 0),), 1)
    framed = jnp.pad(framed, ((0, 0), (1, 1), (1, 1), (0, 0)))
    fine_full = fine_stacked(framed, delta)
    fine_share = space_share(pair_sum(fine_full, core, groups), parts)
    both = jnp.stack([fine_share, coarse_share], axis=0) * scaling
    for bit in (2, 4, 8):
        both = both + lax.ppermute(both, "dp", [(i, i ^ bit) for i in range(groups)])
    other = lax.ppermute(both, "dp", [(i, i ^ 1) for i in range(groups)])
    low = jnp.where(core == 0, both, other)
    high = jnp.where(core == 0, other, both)
    total = jnp.concatenate([low, high], axis=2)
    shape = (total.shape[1],) + fine_full.shape[1:]
    return (total[0].reshape(shape), total[1].reshape(shape))


def solution(mesh):
    placed = (
        P("dp", "space", None, None, None),
        P("dp", "space", None, None, None),
        P("space", None, None, None, None),
        P("dp", None, None, None, "space"),
    )
    return jax.shard_map(
        staged,
        mesh=mesh,
        in_specs=placed,
        out_specs=(P("space", None, None, None, None), P("space", None, None, None, None)),
        check_vma=False,
    )
```
